256 devices in a mesh: gx: 4 (over x_hi, core), gy: 8 (over z), gz: 8 (over x_lo, y).
Axes of the slice: x: 4 (x_hi: 2, x_lo: 2; x = x_hi * 2 + x_lo), y: 4, z: 8, core: 2. Of those that a mesh axis runs over, the one named last changes fastest.
Arguments:
- species: float32 [4, 64, 256, 1024], P(None, 'gx', 'gy', 'gz'), may hold values from -6 to 6
- velocity: float32 [3, 64, 256, 1024], P(None, 'gx', 'gy', 'gz'), may hold values from -15 to 15
- diffusivity: float32 [64, 256, 1024], P('gx', 'gy', 'gz'), may hold values from 0.05 to 1
- reaction: float32 [4, 4], replicated, may hold values from -8 to 8
Outputs:
- updated: float32 [4, 64, 256, 1024], P(None, 'gx', 'gy', 'gz')
- gram: float32 [256, 256], P('gx', 'gz')
The draws below stay inside these ranges and needn't reach their ends.
All inputs are finite; a program needn't handle non-finite values. Where the reference program divides by a largest or mean magnitude, that divisor is 1e-20 or more.
Results may differ from the reference program's by a relative error of at most 0.000068.
Values sent between devices are 32-bit elements; how exact they have to be, the bound alone decides.
No kernel may reach another device: no remote copies, remote signals or barrier semaphores. Data moves between devices by JAX's collectives and lax.ppermute only.
A program may use at most 64 MiB of HBM per device.

```python
import math
import jax
import jax.numpy as jnp
from jax import lax

NS = 4
NX = 64
NY = 256
NZ = 1024


def rolled_ramp(key, length):
    offset = jax.random.randint(key, (), 0, length, dtype=jnp.int32)
    places = (jnp.arange(length, dtype=jnp.int32) + offset) % length
    return places.astype(jnp.float32) / float(length)


def draw_velocity(key, part):
    along_x = rolled_ramp(jax.random.fold_in(key, 11), NX)
    along_y = rolled_ramp(jax.random.fold_in(key, 13), NY)
    along_z = rolled_ramp(jax.random.fold_in(key, 17), NZ)
    grade = 1.0 + 2.0 / 3.0 * (along_x[:, None, None] + along_y[None, :, None] + along_z[None, None, :])
    amplitude = jax.random.uniform(jax.random.fold_in(key, 19), (), jnp.float32, 0.6, 1.0)
    base_key = jax.random.fold_in(key, 23)
    base = jnp.clip(jax.random.normal(base_key, (3, NX, NY, NZ), jnp.float32), -5.0, 5.0)
    return base * (amplitude * grade)[None]


def shard_levels(key, shape, pieces, least, high):
    gain = 1.0
    for dim, blocks in pieces:
        draws = jax.random.uniform(jax.random.fold_in(jax.random.fold_in(key, 6), dim), (blocks,), jnp.float32, least / len(pieces), high / len(pieces))
        gain = gain * jnp.repeat(jnp.exp(draws), shape[dim] // blocks).reshape((-1,) + (1,) * (len(shape) - 1 - dim))
    return gain


def bell_draw(own_key, extent, deviation, limit, shards=(), kind=jnp.bfloat16):
    loudness = shard_levels(own_key, extent, shards, -0.22, 0.18) if shards else 1.0
    entries = jax.random.normal(own_key, extent, jnp.float32) * deviation * loudness
    return jnp.minimum(jnp.maximum(entries, -limit), limit).astype(kind)


def setup_inputs(seed: int = 0) -> dict:
    key_list = jax.random.split(jax.random.key(seed), 5)
    species = bell_draw(key_list[0], (NS, NX, NY, NZ), 1.0, 6.0, ((1, 4), (2, 8), (3, 8)), jnp.float32)
    velocity = draw_velocity(jax.random.fold_in(key_list[4], 71), 0)
    diffusivity = jnp.clip(jnp.exp(math.log(1.0) - 2.9957323 * jax.random.uniform(key_list[2], (NX, NY, NZ), jnp.float32) ** shard_levels(key_list[2], (NX, NY, NZ), ((0, 4), (1, 8), (2, 8)), -0.2, 0.2)), 0.05, 1.0)
    reaction = bell_draw(key_list[3], (NS, NS), 2.0, 8.0, (), jnp.float32)
    return dict(species=species, velocity=velocity, diffusivity=diffusivity, reaction=reaction)


first_coeffs = (4.0 / 5.0, -1.0 / 5.0, 4.0 / 105.0, -1.0 / 280.0)
second_coeffs = (8.0 / 5.0, -1.0 / 5.0, 8.0 / 315.0, -1.0 / 560.0)
centre_weight = -205.0 / 72.0
courant = 0.8


def reference(species, velocity, diffusivity, reaction):
    fastest = jnp.max(jnp.abs(velocity[0]) + jnp.abs(velocity[1]) + jnp.abs(velocity[2]))
    time_step = courant / fastest
    tendency = jnp.einsum("kj,jxyz->kxyz", reaction, species, precision=lax.Precision.HIGHEST)
    for direction in range(3):
        dimension = direction + 1
        first_der = jnp.zeros_like(species)
        second_der = centre_weight * species
        for reach in range(1, 5):
            ahead = jnp.roll(species, -reach, dimension)
            behind = jnp.roll(species, reach, dimension)
            first_der = first_der + first_coeffs[reach - 1] * (ahead - behind)
            second_der = second_der + second_coeffs[reach - 1] * (ahead + behind)
        tendency = tendency - velocity[direction] * first_der + diffusivity * second_der
    updated = species + time_step * tendency
    unfolding = jnp.transpose(updated, (1, 0, 2, 3)).reshape(NX * NS, NY * NZ)
    gram = jnp.dot(unfolding, unfolding.T, precision=lax.Precision.HIGHEST, preferred_element_type=jnp.float32)
    gram = gram / float(NY * NZ)
    return updated, gram
```

```python
import jax
import jax.numpy as jnp
from jax import lax
from jax.sharding import PartitionSpec as P

first_coeffs = (4.0 / 5.0, -1.0 / 5.0, 4.0 / 105.0, -1.0 / 280.0)
second_coeffs = (8.0 / 5.0, -1.0 / 5.0, 8.0 / 315.0, -1.0 / 560.0)
centre_weight = -205.0 / 72.0
courant = 0.8
width = 4


def halos(x, axis, dim):
    peers, length = (lax.axis_size(axis), x.shape[dim])
    up = [(i, (i + 1) % peers) for i in range(peers)]
    down = [(j, i) for i, j in up]
    last = lax.slice_in_dim(x, length - width, length, axis=dim)
    initial = lax.slice_in_dim(x, 0, width, axis=dim)
    before = lax.ppermute(last, axis, up)
    after = lax.ppermute(initial, axis, down)
    return jnp.concatenate([before, x, after], axis=dim)


def body(species, velocity, diffusivity, reaction):
    local_speed = jnp.max(jnp.abs(velocity[0]) + jnp.abs(velocity[1]) + jnp.abs(velocity[2]))
    everyone = ("gx", "gy", "gz")
    slot = lax.axis_index(everyone)
    places = lax.broadcasted_iota(jnp.int32, (128, 128), 0) * 128 + lax.broadcasted_iota(jnp.int32, (128, 128), 1)
    slots = jnp.where(places == slot, local_speed, 0.0)
    fastest = jnp.max(lax.psum(slots, everyone))
    time_step = courant / fastest
    padded = [halos(species, axis, dim) for axis, dim in (("gx", 1), ("gy", 2), ("gz", 3))]
    cells = species.shape[1:]
    tendency = jnp.einsum("kj,jxyz->kxyz", reaction, species, precision=lax.Precision.HIGHEST)
    for direction in range(3):
        dimension = direction + 1
        along = padded[direction]

        def shifted(offset):
            return lax.slice_in_dim(along, width + offset, width + offset + cells[direction], axis=dimension)

        first_der = jnp.zeros_like(species)
        second_der = centre_weight * species
        for reach in range(1, 5):
            ahead = shifted(reach)
            behind = shifted(-reach)
            first_der = first_der + first_coeffs[reach - 1] * (ahead - behind)
            second_der = second_der + second_coeffs[reach - 1] * (ahead + behind)
        tendency = tendency - velocity[direction] * first_der + diffusivity * second_der
    updated = species + time_step * tendency
    nspec = species.shape[0]
    cells_x, cells_y, cells_z = cells
    unfolding = jnp.transpose(updated, (1, 0, 2, 3)).reshape(cells_x * nspec, cells_y * cells_z)
    partial_gram = jnp.dot(
        unfolding,
        lax.all_gather(unfolding, "gx", axis=0, tiled=True).T,
        precision=lax.Precision.HIGHEST,
        preferred_element_type=jnp.float32,
    )
    count_y = lax.axis_size("gy")
    count_z = lax.axis_size("gz")
    summed_all = lax.psum(partial_gram, ("gy", "gz"))
    owned = summed_all.shape[1] // count_z
    summed = lax.dynamic_slice_in_dim(summed_all, lax.axis_index("gz") * owned, owned, axis=1)
    columns_all = float(cells_y * cells_z * count_y * count_z)
    gram = summed / columns_all
    return (updated, gram)


def solution(mesh):
    placed = (P(None, "gx", "gy", "gz"), P(None, "gx", "gy", "gz"), P("gx", "gy", "gz"), P())
    return jax.shard_map(
        body,
        mesh=mesh,
        in_specs=placed,
        out_specs=(P(None, "gx", "gy", "gz"), P("gx", "gz")),
        check_vma=False,
    )
```

```python
import jax
import jax.numpy as jnp
from jax import lax
from jax.sharding import PartitionSpec as P

first_coeffs = (4.0 / 5.0, -1.0 / 5.0, 4.0 / 105.0, -1.0 / 280.0)
second_coeffs = (8.0 / 5.0, -1.0 / 5.0, 8.0 / 315.0, -1.0 / 560.0)
centre_weight = -205.0 / 72.0
courant = 0.8
width = 4


def halos(x, axis, dim):
    peers, length = (lax.axis_size(axis), x.shape[dim])
    up = [(i, (i + 1) % peers) for i in range(peers)]
    down = [(j, i) for i, j in up]
    last = lax.slice_in_dim(x, length - width, length, axis=dim)
    initial = lax.slice_in_dim(x, 0, width, axis=dim)
    before = lax.ppermute(last, axis, up)
    after = lax.ppermute(initial, axis, down)
    return jnp.concatenate([before, x, after], axis=dim)


def partners(axis, bit):
    return [(i, i ^ bit) for i in range(lax.axis_size(axis))]


def butterfly_max(value, axis):
    bit = 1
    while bit < lax.axis_size(axis):
        value = jnp.maximum(value, lax.ppermute(value, axis, partners(axis, bit)))
        bit *= 2
    return value


def scatter_over_gz(partial):
    peers = lax.axis_size("gz")
    me = lax.axis_index("gz")
    part = partial
    bit = peers // 2
    while bit >= 1:
        half = part.shape[1] // 2
        low, high = part[:, :half], part[:, half:]
        upper = (me & bit) != 0
        keep = jnp.where(upper, high, low)
        send = jnp.where(upper, low, high)
        part = keep + lax.ppermute(send, "gz", partners("gz", bit))
        bit //= 2
    return part


def sum_over_gy(part):
    bit = 1
    while bit < lax.axis_size("gy"):
        part = part + lax.ppermute(part, "gy", partners("gy", bit))
        bit *= 2
    return part


def body(species, velocity, diffusivity, reaction):
    local_speed = jnp.max(jnp.abs(velocity[0]) + jnp.abs(velocity[1]) + jnp.abs(velocity[2]))
    fastest = local_speed
    for axis in ("gx", "gy", "gz"):
        fastest = butterfly_max(fastest, axis)
    time_step = courant / fastest
    padded = [halos(species, axis, dim) for axis, dim in (("gx", 1), ("gy", 2), ("gz", 3))]
    cells = species.shape[1:]
    tendency = jnp.einsum("kj,jxyz->kxyz", reaction, species, precision=lax.Precision.HIGHEST)
    for direction in range(3):
        dimension = direction + 1
        along = padded[direction]

        def shifted(offset):
            return lax.slice_in_dim(along, width + offset, width + offset + cells[direction], axis=dimension)

        first_der = jnp.zeros_like(species)
        second_der = centre_weight * species
        for reach in range(1, 5):
            ahead = shifted(reach)
            behind = shifted(-reach)
            first_der = first_der + first_coeffs[reach - 1] * (ahead - behind)
            second_der = second_der + second_coeffs[reach - 1] * (ahead + behind)
        tendency = tendency - velocity[direction] * first_der + diffusivity * second_der
    updated = species + time_step * tendency
    nspec = species.shape[0]
    cells_x, cells_y, cells_z = cells
    unfolding = jnp.transpose(updated, (1, 0, 2, 3)).reshape(cells_x * nspec, cells_y * cells_z)
    partial_gram = jnp.dot(
        unfolding,
        lax.all_gather(unfolding, "gx", axis=0, tiled=True).T,
        precision=lax.Precision.HIGHEST,
        preferred_element_type=jnp.float32,
    )
    count_y = lax.axis_size("gy")
    count_z = lax.axis_size("gz")
    summed = sum_over_gy(scatter_over_gz(partial_gram))
    columns_all = float(cells_y * cells_z * count_y * count_z)
    gram = summed / columns_all
    return (updated, gram)


def solution(mesh):
    placed = (P(None, "gx", "gy", "gz"), P(None, "gx", "gy", "gz"), P("gx", "gy", "gz"), P())
    return jax.shard_map(
        body,
        mesh=mesh,
        in_specs=placed,
        out_specs=(P(None, "gx", "gy", "gz"), P("gx", "gz")),
        check_vma=False,
    )
```

```python
import jax
import jax.numpy as jnp
from jax import lax
from jax.sharding import PartitionSpec as P

first_coeffs = (4.0 / 5.0, -1.0 / 5.0, 4.0 / 105.0, -1.0 / 280.0)
second_coeffs = (8.0 / 5.0, -1.0 / 5.0, 8.0 / 315.0, -1.0 / 560.0)
centre_weight = -205.0 / 72.0
courant = 0.8
width = 4


def halos(x, axis, dim):
    peers, length = (lax.axis_size(axis), x.shape[dim])
    up = [(i, (i + 1) % peers) for i in range(peers)]
    down = [(j, i) for i, j in up]
    last = lax.slice_in_dim(x, length - width, length, axis=dim)
    initial = lax.slice_in_dim(x, 0, width, axis=dim)
    before = lax.ppermute(last, axis, up)
    after = lax.ppermute(initial, axis, down)
    return jnp.concatenate([before, x, after], axis=dim)


def shifts(axis):
    peers = lax.axis_size(axis)
    return [[(i, (i + s) % peers) for i in range(peers)] for s in range(1, peers)]


def spread_max(value, axis):
    best = value
    for pairs in shifts(axis):
        best = jnp.maximum(best, lax.ppermute(value, axis, pairs))
    return best


def partners(axis, bit):
    return [(i, i ^ bit) for i in range(lax.axis_size(axis))]


def butterfly_max(value, axis):
    bit = 1
    while bit < lax.axis_size(axis):
        value = jnp.maximum(value, lax.ppermute(value, axis, partners(axis, bit)))
        bit *= 2
    return value


def scatter_over_gz(partial):
    peers = lax.axis_size("gz")
    me = lax.axis_index("gz")
    part = partial
    bit = peers // 2
    while bit >= 1:
        half = part.shape[1] // 2
        low, high = part[:, :half], part[:, half:]
        upper = (me & bit) != 0
        keep = jnp.where(upper, high, low)
        send = jnp.where(upper, low, high)
        part = keep + lax.ppermute(send, "gz", partners("gz", bit))
        bit //= 2
    return part


def sum_over_gy(part):
    bit = 1
    while bit < lax.axis_size("gy"):
        part = part + lax.ppermute(part, "gy", partners("gy", bit))
        bit *= 2
    return part


def body(species, velocity, diffusivity, reaction):
    local_speed = jnp.max(jnp.abs(velocity[0]) + jnp.abs(velocity[1]) + jnp.abs(velocity[2]))
    fastest = local_speed
    for axis in ("gx", "gy", "gz"):
        fastest = spread_max(fastest, axis)
    time_step = courant / fastest
    padded = [halos(species, axis, dim) for axis, dim in (("gx", 1), ("gy", 2), ("gz", 3))]
    cells = species.shape[1:]
    tendency = jnp.einsum("kj,jxyz->kxyz", reaction, species, precision=lax.Precision.HIGHEST)
    for direction in range(3):
        dimension = direction + 1
        along = padded[direction]

        def shifted(offset):
            return lax.slice_in_dim(along, width + offset, width + offset + cells[direction], axis=dimension)

        first_der = jnp.zeros_like(species)
        second_der = centre_weight * species
        for reach in range(1, 5):
            ahead = shifted(reach)
            behind = shifted(-reach)
            first_der = first_der + first_coeffs[reach - 1] * (ahead - behind)
            second_der = second_der + second_coeffs[reach - 1] * (ahead + behind)
        tendency = tendency - velocity[direction] * first_der + diffusivity * second_der
    updated = species + time_step * tendency
    nspec = species.shape[0]
    cells_x, cells_y, cells_z = cells
    unfolding = jnp.transpose(updated, (1, 0, 2, 3)).reshape(cells_x * nspec, cells_y * cells_z)
    partial_gram = jnp.dot(
        unfolding,
        lax.all_gather(unfolding, "gx", axis=0, tiled=True).T,
        precision=lax.Precision.HIGHEST,
        preferred_element_type=jnp.float32,
    )
    count_y = lax.axis_size("gy")
    count_z = lax.axis_size("gz")
    summed = sum_over_gy(scatter_over_gz(partial_gram))
    columns_all = float(cells_y * cells_z * count_y * count_z)
    gram = summed / columns_all
    return (updated, gram)


def solution(mesh):
    placed = (P(None, "gx", "gy", "gz"), P(None, "gx", "gy", "gz"), P("gx", "gy", "gz"), P())
    return jax.shard_map(
        body,
        mesh=mesh,
        in_specs=placed,
        out_specs=(P(None, "gx", "gy", "gz"), P("gx", "gz")),
        check_vma=False,
    )
```

```python
import jax
import jax.numpy as jnp
from jax import lax
from jax.sharding import PartitionSpec as P

first_coeffs = (4.0 / 5.0, -1.0 / 5.0, 4.0 / 105.0, -1.0 / 280.0)
second_coeffs = (8.0 / 5.0, -1.0 / 5.0, 8.0 / 315.0, -1.0 / 560.0)
centre_weight = -205.0 / 72.0
courant = 0.8
width = 4


def halos(x, axis, dim):
    peers, length = (lax.axis_size(axis), x.shape[dim])
    up = [(i, (i + 1) % peers) for i in range(peers)]
    down = [(j, i) for i, j in up]
    last = lax.slice_in_dim(x, length - width, length, axis=dim)
    initial = lax.slice_in_dim(x, 0, width, axis=dim)
    before = lax.ppermute(last, axis, up)
    after = lax.ppermute(initial, axis, down)
    return jnp.concatenate([before, x, after], axis=dim)


def partners(axis, bit):
    return [(i, i ^ bit) for i in range(lax.axis_size(axis))]


def butterfly_max(value, axis):
    bit = 1
    while bit < lax.axis_size(axis):
        value = jnp.maximum(value, lax.ppermute(value, axis, partners(axis, bit)))
        bit *= 2
    return value


def scatter_over_gz(partial):
    peers = lax.axis_size("gz")
    me = lax.axis_index("gz")
    part = partial
    bit = peers // 2
    while bit >= 1:
        half = part.shape[1] // 2
        low, high = part[:, :half], part[:, half:]
        upper = (me & bit) != 0
        keep = jnp.where(upper, high, low)
        send = jnp.where(upper, low, high)
        part = keep + lax.ppermute(send, "gz", partners("gz", bit))
        bit //= 2
    return part


def sum_over_gy(part):
    bit = 1
    while bit < lax.axis_size("gy"):
        part = part + lax.ppermute(part, "gy", partners("gy", bit))
        bit *= 2
    return part


def body(species, velocity, diffusivity, reaction):
    speed = jnp.abs(velocity[0]) + jnp.abs(velocity[1]) + jnp.abs(velocity[2])
    lanes = speed.shape[-1]
    tile = jnp.max(speed.reshape(-1, 8, lanes), axis=0)
    fastest = jnp.max(lax.all_gather(tile, ("gx", "gy", "gz"), axis=0, tiled=True))
    time_step = courant / fastest
    padded = [halos(species, axis, dim) for axis, dim in (("gx", 1), ("gy", 2), ("gz", 3))]
    cells = species.shape[1:]
    tendency = jnp.einsum("kj,jxyz->kxyz", reaction, species, precision=lax.Precision.HIGHEST)
    for direction in range(3):
        dimension = direction + 1
        along = padded[direction]

        def shifted(offset):
            return lax.slice_in_dim(along, width + offset, width + offset + cells[direction], axis=dimension)

        first_der = jnp.zeros_like(species)
        second_der = centre_weight * species
        for reach in range(1, 5):
            ahead = shifted(reach)
            behind = shifted(-reach)
            first_der = first_der + first_coeffs[reach - 1] * (ahead - behind)
            second_der = second_der + second_coeffs[reach - 1] * (ahead + behind)
        tendency = tendency - velocity[direction] * first_der + diffusivity * second_der
    tendency = lax.optimization_barrier(tendency)
    updated = species + time_step * tendency
    nspec = species.shape[0]
    cells_x, cells_y, cells_z = cells
    unfolding = jnp.transpose(updated, (1, 0, 2, 3)).reshape(cells_x * nspec, cells_y * cells_z)
    partial_gram = jnp.dot(
        unfolding,
        lax.all_gather(unfolding, "gx", axis=0, tiled=True).T,
        precision=lax.Precision.HIGHEST,
        preferred_element_type=jnp.float32,
    )
    count_y = lax.axis_size("gy")
    count_z = lax.axis_size("gz")
    summed = sum_over_gy(scatter_over_gz(partial_gram))
    columns_all = float(cells_y * cells_z * count_y * count_z)
    gram = summed / columns_all
    return (updated, gram)


def solution(mesh):
    placed = (P(None, "gx", "gy", "gz"), P(None, "gx", "gy", "gz"), P("gx", "gy", "gz"), P())
    return jax.shard_map(
        body,
        mesh=mesh,
        in_specs=placed,
        out_specs=(P(None, "gx", "gy", "gz"), P("gx", "gz")),
        check_vma=False,
    )
```

```python
import jax
import jax.numpy as jnp
from jax import lax
from jax.sharding import PartitionSpec as P

first_coeffs = (4.0 / 5.0, -1.0 / 5.0, 4.0 / 105.0, -1.0 / 280.0)
second_coeffs = (8.0 / 5.0, -1.0 / 5.0, 8.0 / 315.0, -1.0 / 560.0)
centre_weight = -205.0 / 72.0
courant = 0.8
width = 4


def halos(x, axis, dim):
    peers, length = (lax.axis_size(axis), x.shape[dim])
    up = [(i, (i + 1) % peers) for i in range(peers)]
    down = [(j, i) for i, j in up]
    last = lax.slice_in_dim(x, length - width, length, axis=dim)
    initial = lax.slice_in_dim(x, 0, width, axis=dim)
    before = lax.ppermute(last, axis, up)
    after = lax.ppermute(initial, axis, down)
    return jnp.concatenate([before, x, after], axis=dim)


def partners(axis, bit):
    return [(i, i ^ bit) for i in range(lax.axis_size(axis))]


def butterfly_max(value, axis):
    bit = 1
    while bit < lax.axis_size(axis):
        value = jnp.maximum(value, lax.ppermute(value, axis, partners(axis, bit)))
        bit *= 2
    return value


def scatter_over_gz(partial):
    peers = lax.axis_size("gz")
    me = lax.axis_index("gz")
    part = partial
    bit = peers // 2
    while bit >= 1:
        half = part.shape[1] // 2
        low, high = part[:, :half], part[:, half:]
        upper = (me & bit) != 0
        keep = jnp.where(upper, high, low)
        send = jnp.where(upper, low, high)
        part = keep + lax.ppermute(send, "gz", partners("gz", bit))
        bit //= 2
    return part


def sum_over_gy(part):
    bit = 1
    while bit < lax.axis_size("gy"):
        part = part + lax.ppermute(part, "gy", partners("gy", bit))
        bit *= 2
    return part


def product(a, b):
    return jnp.dot(a, b.T, precision=lax.Precision.HIGHEST, preferred_element_type=jnp.float32)


def rows_against_all(rows):
    if lax.axis_size("gx") != 4:
        everyone = lax.all_gather(rows, "gx", axis=0, tiled=True)
        return product(rows, everyone)
    me = lax.axis_index("gx")
    across = [(0, 2), (1, 3), (2, 1), (3, 0)]
    back = [(j, i) for i, j in across]
    source = jnp.array([3, 2, 0, 1])[me]
    target = jnp.array([2, 3, 1, 0])[me]
    mate = lax.ppermute(rows, "gx", [(i, i ^ 1) for i in range(4)])
    far = lax.ppermute(rows, "gx", across)
    own = product(rows, rows)
    with_mate = product(rows, mate)
    with_far = product(rows, far)
    returned = lax.ppermute(with_far.T, "gx", back)
    blocks = []
    for h in range(4):
        block = jnp.where(h == target, returned, with_far)
        block = jnp.where(h == me ^ 1, with_mate, block)
        block = jnp.where(h == me, own, block)
        blocks.append(block)
    return jnp.concatenate(blocks, axis=1)


def body(species, velocity, diffusivity, reaction):
    local_speed = jnp.max(jnp.abs(velocity[0]) + jnp.abs(velocity[1]) + jnp.abs(velocity[2]))
    fastest = local_speed
    for axis in ("gx", "gy", "gz"):
        fastest = butterfly_max(fastest, axis)
    time_step = courant / fastest
    padded = [halos(species, axis, dim) for axis, dim in (("gx", 1), ("gy", 2), ("gz", 3))]
    cells = species.shape[1:]
    tendency = jnp.einsum("kj,jxyz->kxyz", reaction, species, precision=lax.Precision.HIGHEST)
    for direction in range(3):
        dimension = direction + 1
        along = padded[direction]

        def shifted(offset):
            return lax.slice_in_dim(along, width + offset, width + offset + cells[direction], axis=dimension)

        first_der = jnp.zeros_like(species)
        second_der = centre_weight * species
        for reach in range(1, 5):
            ahead = shifted(reach)
            behind = shifted(-reach)
            first_der = first_der + first_coeffs[reach - 1] * (ahead - behind)
            second_der = second_der + second_coeffs[reach - 1] * (ahead + behind)
        tendency = tendency - velocity[direction] * first_der + diffusivity * second_der
    updated = species + time_step * tendency
    nspec = species.shape[0]
    cells_x, cells_y, cells_z = cells
    unfolding = jnp.transpose(updated, (1, 0, 2, 3)).reshape(cells_x * nspec, cells_y * cells_z)
    partial_gram = rows_against_all(unfolding)
    count_y = lax.axis_size("gy")
    count_z = lax.axis_size("gz")
    summed = sum_over_gy(scatter_over_gz(partial_gram))
    columns_all = float(cells_y * cells_z * count_y * count_z)
    gram = summed / columns_all
    return (updated, gram)


def solution(mesh):
    placed = (P(None, "gx", "gy", "gz"), P(None, "gx", "gy", "gz"), P("gx", "gy", "gz"), P())
    return jax.shard_map(
        body,
        mesh=mesh,
        in_specs=placed,
        out_specs=(P(None, "gx", "gy", "gz"), P("gx", "gz")),
        check_vma=False,
    )
```
